256 devices in a mesh: pair: 16 (over z, core), virt: 16 (over x, y).
Axes of the slice: x: 4, y: 4, z: 8, core: 2. Of those that a mesh axis runs over, the one named last changes fastest.
Arguments:
- amplitudes: float32 [64, 2048, 4096], P('virt', 'pair'), may hold values from -0.9 to 0.9
- integrals: float32 [64, 384, 4096], P('virt', 'pair'), may hold values from -0.09375 to 0.09375
- tile_flags: int32 [64], P('virt'), may hold values 0 or 1
- live_count: int32 [16], replicated, may hold values from 1 to 4, as said below
- pair_occ: int32 [2048, 2], P(('pair', 'virt')), may hold values from 0 to 199
- occ_energy: float32 [200], replicated, may hold values from -2.5 to -0.3
- ab_energy: float32 [384], replicated, may hold values from 0.6 to 3
Outputs:
- ladder: float32 [2048, 384], P(('pair', 'virt'))
- update: float32 [2048, 384], P(('pair', 'virt'))
The draws below stay inside these ranges and needn't reach their ends.
Inputs may be any that keep to these rules, and one draw needn't show every extreme that they name: `live_count`: entry v is how many of the 4 slots of virt index v hold tile pairs: its slots below that number do, and the contents of the others are not to be used. At some index it is 4, and at the index half the axis away it is 1.
All inputs are finite; a program needn't handle non-finite values. No bound on the sum of `tile_flags` on one device may be relied on, other than what follows from the above.
Results may differ from the reference program's by a relative error of at most 0.0001.
Values sent between devices are 32-bit elements; how exact they have to be, the bound alone decides.
No kernel may reach another device: no remote copies, remote signals or barrier semaphores. Data moves between devices by JAX's collectives and lax.ppermute only.
A program may use at most 128 MiB of HBM per device.

```python
import jax
import jax.numpy as jnp
from jax import lax

TILE = 64
NOCC = 200
SLOTS = 4
AB = 384
TT = 4096
PAIRS = 2048
TILES = 64
N_VIRT = 16


def draw_live_count(key, part):
    key_one, key_two, key_three = jax.random.split(key, 3)
    first_draw = jax.random.randint(key_one, (N_VIRT,), 1, SLOTS + 1)
    second_draw = jax.random.randint(key_two, (N_VIRT,), 1, SLOTS + 1)
    counts = jnp.minimum(first_draw, second_draw)
    full_index = jax.random.randint(key_three, (), 0, N_VIRT)
    positions = jnp.arange(N_VIRT)
    counts = jnp.where(positions == full_index, SLOTS, counts)
    counts = jnp.where(positions == (full_index + N_VIRT // 2) % N_VIRT, 1, counts)
    return counts.astype(jnp.int32)


def touch_ends(values, rng, smallest, largest):
    place = [jax.random.randint(jax.random.fold_in(rng, axis), (), 0, length) for axis, length in enumerate(values.shape)]
    main_axis = values.shape.index(max(values.shape))
    beside = place[:main_axis] + [(place[main_axis] + 1) % values.shape[main_axis]] + place[main_axis + 1:]
    return values.at[tuple(place)].set(smallest).at[tuple(beside)].set(largest)


def spiked(entries, rng, source, target, parts, factor):
    owner, partner = [(jnp.arange(entries.shape[dim]) // (entries.shape[dim] // parts)).reshape([-1 if axis == dim else 1 for axis in range(entries.ndim)]) for dim in (source, target)]
    chosen = jax.random.permutation(rng, parts)[partner]
    strong = (owner == chosen) | (owner == (partner + parts // 2) % parts)
    return jnp.where(strong, factor * entries, entries)


def shard_levels(rng, extent, pieces, least, top_value):
    def one(axis_at, blocks):
        steps = jax.random.uniform(jax.random.fold_in(jax.random.fold_in(rng, 6), axis_at), (blocks,), jnp.float32, least / len(pieces), top_value / len(pieces))
        return jnp.repeat(jnp.exp(steps), extent[axis_at] // blocks).reshape((-1,) + (1,) * (len(extent) - axis_at - 1))

    loudness = one(*pieces[0])
    for cut in pieces[1:]:
        loudness = loudness * one(*cut)
    return loudness


def scatter_about(key, dims, deviation, limit, shards=(), kind=jnp.bfloat16):
    loudness = shard_levels(key, dims, shards, -0.22, 0.18) if shards else 1.0
    drawn = jax.random.normal(key, dims, jnp.float32) * deviation * loudness
    return jnp.minimum(jnp.maximum(drawn, -limit), limit).astype(kind)


def noise_with(own_key, shape, scale, bound, cuts, heavy, kind=jnp.bfloat16):
    entries = scale * jax.random.normal(own_key, shape, jnp.float32)
    if cuts:
        entries = entries * shard_levels(own_key, shape, cuts, -0.22, 0.18)
    return jnp.clip(spiked(entries, jax.random.fold_in(own_key, 3), *heavy), -bound, bound).astype(kind)


def setup_inputs(seed: int = 0) -> dict:
    key_list = jax.random.split(jax.random.key(seed), 8)
    amplitudes = noise_with(key_list[0], (TILES, PAIRS, TT), 0.15, 0.9, ((0, 16), (1, 16)), (0, 1, 16, 2.0), jnp.float32)
    integrals = scatter_about(key_list[1], (TILES, AB, TT), TT ** -0.5, 0.09375, ((0, 16), (1, 16)), jnp.float32)
    tile_flags = touch_ends((jax.random.randint(key_list[2], (TILES,), 0, 2) < 1).astype(jnp.int32), jax.random.fold_in(key_list[2], 1), 0, 1)
    live_count = draw_live_count(jax.random.fold_in(key_list[7], 71), 0)
    pair_occ = touch_ends(jax.random.randint(key_list[4], (PAIRS, 2), 0, NOCC), jax.random.fold_in(key_list[4], 1), 0, NOCC - 1).astype(jnp.int32)
    occ_energy = jnp.clip(jax.random.uniform(key_list[5], (NOCC,), jnp.float32, -2.5, -0.3), -2.5, -0.3)
    ab_energy = jnp.clip(jax.random.uniform(key_list[6], (AB,), jnp.float32, 0.6, 3.0), 0.6, 3.0)
    return {"amplitudes": amplitudes, "integrals": integrals, "tile_flags": tile_flags, "live_count": live_count, "pair_occ": pair_occ, "occ_energy": occ_energy, "ab_energy": ab_energy}


def symmetric(integrals, tile_flags):
    shaped = integrals.reshape(integrals.shape[0], integrals.shape[1], TILE, TILE)
    swapped = jnp.swapaxes(shaped, 2, 3).reshape(integrals.shape)
    return integrals + tile_flags.astype(jnp.float32)[:, None, None] * swapped


def reference(amplitudes, integrals, tile_flags, live_count, pair_occ, occ_energy, ab_energy):
    slot_index = jnp.arange(TILES, dtype=jnp.int32)
    live_mask = ((slot_index % SLOTS) < live_count[slot_index // SLOTS]).astype(jnp.float32)
    sym_integrals = symmetric(integrals, tile_flags)

    def one_tile(running, tile_items):
        amp_tile, int_tile, weight = tile_items
        tile_term = lax.dot_general(amp_tile, int_tile, (((1,), (1,)), ((), ())),
                                    precision=lax.Precision.HIGHEST,
                                    preferred_element_type=jnp.float32)
        return running + weight * tile_term, None

    ladder = lax.scan(one_tile, jnp.zeros((PAIRS, AB), jnp.float32),
                      (amplitudes, sym_integrals, live_mask))[0]
    first_energy = occ_energy[pair_occ[:, 0]]
    second_energy = occ_energy[pair_occ[:, 1]]
    denominator = ab_energy[None, :] - first_energy[:, None] - second_energy[:, None]
    return ladder, ladder / denominator
```

```python
import jax
import jax.numpy as jnp
from jax import lax
from jax.sharding import PartitionSpec as P

TILE = 64


def symmetric_rows(rows, flag):
    shaped = rows.reshape(rows.shape[0], TILE, TILE)
    swapped = jnp.swapaxes(shaped, 1, 2).reshape(rows.shape)
    return rows + flag.astype(jnp.float32) * swapped


def tile_product(amp_tile, int_rows):
    return lax.dot_general(
        amp_tile,
        int_rows,
        (((1,), (1,)), ((), ())),
        precision=lax.Precision.HIGHEST,
        preferred_element_type=jnp.float32,
    )


def on_device(amplitudes, integrals, tile_flags, live_count, pair_occ, occ_energy, ab_energy):
    slots, pair_rows, _ = amplitudes.shape
    virt_index = lax.axis_index("virt")
    n_virt = lax.axis_size("virt")
    own_count = live_count[virt_index]

    running = None
    for slot in range(slots):
        sym_rows = symmetric_rows(integrals[slot], tile_flags[slot])
        gathered = lax.all_gather(sym_rows, "pair", axis=0, tiled=True)
        term = tile_product(amplitudes[slot], gathered)
        term = jnp.where(slot < own_count, term, jnp.zeros_like(term))
        running = term if running is None else running + term

    ab = running.shape[1]
    blocks = running.reshape(n_virt, pair_rows // n_virt, ab)
    received = lax.all_to_all(blocks, "virt", 0, 0, tiled=False)
    ladder = jnp.sum(received, axis=0)

    occ_range = jnp.arange(occ_energy.shape[0], dtype=jnp.int32)
    first_energy = jnp.sum(
        jnp.where(pair_occ[:, 0:1] == occ_range[None, :], occ_energy[None, :], 0.0), axis=1
    )
    second_energy = jnp.sum(
        jnp.where(pair_occ[:, 1:2] == occ_range[None, :], occ_energy[None, :], 0.0), axis=1
    )
    denominator = ab_energy[None, :] - first_energy[:, None] - second_energy[:, None]
    return (ladder, ladder / denominator)


def solution(mesh):
    return jax.shard_map(
        on_device,
        mesh=mesh,
        in_specs=(
            P("virt", "pair", None),
            P("virt", "pair", None),
            P("virt"),
            P(),
            P(("pair", "virt"), None),
            P(),
            P(),
        ),
        out_specs=(P(("pair", "virt"), None), P(("pair", "virt"), None)),
        check_vma=False,
    )
```

```python
import jax
import jax.numpy as jnp
from jax import lax
from jax.sharding import PartitionSpec as P

TILE = 64


def swap_in_tile(rows):
    shaped = rows.reshape(rows.shape[0], TILE, TILE)
    return jnp.swapaxes(shaped, 1, 2).reshape(rows.shape)


def symmetric_amps(amp_rows, flag):
    return amp_rows + flag.astype(jnp.float32) * swap_in_tile(amp_rows)


def tile_product(amp_tile, int_rows):
    return lax.dot_general(
        amp_tile,
        int_rows,
        (((1,), (1,)), ((), ())),
        precision=lax.Precision.HIGHEST,
        preferred_element_type=jnp.float32,
    )


def on_device(amplitudes, integrals, tile_flags, live_count, pair_occ, occ_energy, ab_energy):
    slots, pair_rows, _ = amplitudes.shape
    n_virt = lax.axis_size("virt")
    half = n_virt // 2
    virt_index = lax.axis_index("virt")
    partner = (virt_index + half) % n_virt
    own_count = live_count[virt_index]
    partner_count = live_count[partner]
    give = jnp.clip((own_count - partner_count) // 2, 0, 1)
    take = jnp.clip((partner_count - own_count) // 2, 0, 1)
    keep = own_count - give
    work = keep + take

    send_at = own_count - 1
    send_amp = symmetric_amps(
        lax.dynamic_index_in_dim(amplitudes, send_at, 0, keepdims=False),
        lax.dynamic_index_in_dim(tile_flags, send_at, 0, keepdims=False),
    )
    send_int = lax.dynamic_index_in_dim(integrals, send_at, 0, keepdims=False)
    perm = [(v, (v + half) % n_virt) for v in range(n_virt)]
    recv_int = lax.ppermute(send_int, "virt", perm)
    recv_amp = lax.ppermute(send_amp, "virt", perm)

    def work_rows(slot):
        own_int = integrals[slot]
        own_amp = symmetric_amps(amplitudes[slot], tile_flags[slot])
        if slot == 0:
            return own_int, own_amp
        mine = slot < keep
        return jnp.where(mine, own_int, recv_int), jnp.where(mine, own_amp, recv_amp)

    def slot_term(slot):
        int_rows, amp_rows = work_rows(slot)
        gathered = lax.all_gather(int_rows, "pair", axis=0, tiled=True)
        return tile_product(amp_rows, gathered)

    running = None
    for slot in range(slots - 1):
        term = slot_term(slot)
        term = jnp.where(slot < work, term, jnp.zeros_like(term))
        running = term if running is None else running + term
    last = slots - 1
    running = lax.cond(
        last < work, lambda acc: acc + slot_term(last), lambda acc: acc, running
    )

    ab = running.shape[1]
    blocks = running.reshape(n_virt, pair_rows // n_virt, ab)
    received = lax.all_to_all(blocks, "virt", 0, 0, tiled=False)
    ladder = jnp.sum(received, axis=0)

    occ_range = jnp.arange(occ_energy.shape[0], dtype=jnp.int32)
    first_energy = jnp.sum(
        jnp.where(pair_occ[:, 0:1] == occ_range[None, :], occ_energy[None, :], 0.0), axis=1
    )
    second_energy = jnp.sum(
        jnp.where(pair_occ[:, 1:2] == occ_range[None, :], occ_energy[None, :], 0.0), axis=1
    )
    denominator = ab_energy[None, :] - first_energy[:, None] - second_energy[:, None]
    return (ladder, ladder / denominator)


def solution(mesh):
    return jax.shard_map(
        on_device,
        mesh=mesh,
        in_specs=(
            P("virt", "pair", None),
            P("virt", "pair", None),
            P("virt"),
            P(),
            P(("pair", "virt"), None),
            P(),
            P(),
        ),
        out_specs=(P(("pair", "virt"), None), P(("pair", "virt"), None)),
        check_vma=False,
    )
```

```python
import jax
import jax.numpy as jnp
from jax import lax
from jax.sharding import PartitionSpec as P

TILE = 64


def swap_in_tile(rows):
    shaped = rows.reshape(rows.shape[0], TILE, TILE)
    return jnp.swapaxes(shaped, 1, 2).reshape(rows.shape)


def symmetric_amps(amp_rows, flag):
    return amp_rows + flag.astype(jnp.float32) * swap_in_tile(amp_rows)


def tile_product(amp_tile, int_rows):
    return lax.dot_general(
        amp_tile,
        int_rows,
        (((1,), (1,)), ((), ())),
        precision=lax.Precision.HIGH,
        preferred_element_type=jnp.float32,
    )


def on_device(amplitudes, integrals, tile_flags, live_count, pair_occ, occ_energy, ab_energy):
    slots, pair_rows, _ = amplitudes.shape
    n_virt = lax.axis_size("virt")
    half = n_virt // 2
    virt_index = lax.axis_index("virt")
    partner = (virt_index + half) % n_virt
    own_count = live_count[virt_index]
    partner_count = live_count[partner]
    give = jnp.clip((own_count - partner_count) // 2, 0, 1)
    take = jnp.clip((partner_count - own_count) // 2, 0, 1)
    keep = own_count - give

    send_at = own_count - 1
    send_amp = symmetric_amps(
        lax.dynamic_index_in_dim(amplitudes, send_at, 0, keepdims=False),
        lax.dynamic_index_in_dim(tile_flags, send_at, 0, keepdims=False),
    )
    send_int = lax.dynamic_index_in_dim(integrals, send_at, 0, keepdims=False)
    perm = [(v, (v + half) % n_virt) for v in range(n_virt)]
    recv_int = lax.ppermute(send_int, "virt", perm)
    recv_amp = lax.ppermute(send_amp, "virt", perm)

    def own_amps(slot):
        return symmetric_amps(amplitudes[slot], tile_flags[slot])

    first_two = lax.all_gather(integrals[0:2], "pair", axis=1, tiled=True)
    running = tile_product(own_amps(0), first_two[0])
    second = tile_product(own_amps(1), first_two[1])
    running = running + jnp.where(keep > 1, second, jnp.zeros_like(second))

    third_int = jnp.where(take > 0, recv_int, integrals[2])
    third_amp = jnp.where(take > 0, recv_amp, own_amps(2))
    third = tile_product(third_amp, lax.all_gather(third_int, "pair", axis=0, tiled=True))
    third_live = (take > 0) | (keep > 2)
    running = running + jnp.where(third_live, third, jnp.zeros_like(third))

    def fourth(acc):
        gathered = lax.all_gather(integrals[3], "pair", axis=0, tiled=True)
        return acc + tile_product(own_amps(3), gathered)

    all_counts = live_count
    all_partners = jnp.roll(live_count, half)
    all_keep = all_counts - jnp.clip((all_counts - all_partners) // 2, 0, 1)
    any_full = jnp.max(all_keep) > 3
    with_fourth = lax.cond(any_full, fourth, lambda acc: acc, running)
    running = jnp.where(keep > 3, with_fourth, running)

    ab = running.shape[1]
    blocks = running.reshape(n_virt, pair_rows // n_virt, ab)
    received = lax.all_to_all(blocks, "virt", 0, 0, tiled=False)
    ladder = jnp.sum(received, axis=0)

    occ_range = jnp.arange(occ_energy.shape[0], dtype=jnp.int32)
    first_energy = jnp.sum(
        jnp.where(pair_occ[:, 0:1] == occ_range[None, :], occ_energy[None, :], 0.0), axis=1
    )
    second_energy = jnp.sum(
        jnp.where(pair_occ[:, 1:2] == occ_range[None, :], occ_energy[None, :], 0.0), axis=1
    )
    denominator = ab_energy[None, :] - first_energy[:, None] - second_energy[:, None]
    return (ladder, ladder / denominator)


def solution(mesh):
    return jax.shard_map(
        on_device,
        mesh=mesh,
        in_specs=(
            P("virt", "pair", None),
            P("virt", "pair", None),
            P("virt"),
            P(),
            P(("pair", "virt"), None),
            P(),
            P(),
        ),
        out_specs=(P(("pair", "virt"), None), P(("pair", "virt"), None)),
        check_vma=False,
    )
```

```python
import jax
import jax.numpy as jnp
from jax import lax
from jax.sharding import PartitionSpec as P

TILE = 64


def swap_in_tile(rows):
    shaped = rows.reshape(rows.shape[0], TILE, TILE)
    return jnp.swapaxes(shaped, 1, 2).reshape(rows.shape)


def symmetric_amps(amp_rows, flag):
    return amp_rows + flag.astype(jnp.float32) * swap_in_tile(amp_rows)


def tile_product(amp_tile, int_rows, precision=lax.Precision.HIGH):
    return lax.dot_general(
        amp_tile,
        int_rows,
        (((1,), (1,)), ((), ())),
        precision=precision,
        preferred_element_type=jnp.float32,
    )


def on_device(amplitudes, integrals, tile_flags, live_count, pair_occ, occ_energy, ab_energy):
    slots, pair_rows, _ = amplitudes.shape
    n_virt = lax.axis_size("virt")
    half = n_virt // 2
    virt_index = lax.axis_index("virt")
    partner = (virt_index + half) % n_virt
    own_count = live_count[virt_index]
    partner_count = live_count[partner]
    give = jnp.clip((own_count - partner_count) // 2, 0, 1)
    take = jnp.clip((partner_count - own_count) // 2, 0, 1)
    keep = own_count - give

    send_at = own_count - 1
    send_amp = symmetric_amps(
        lax.dynamic_index_in_dim(amplitudes, send_at, 0, keepdims=False),
        lax.dynamic_index_in_dim(tile_flags, send_at, 0, keepdims=False),
    )
    send_int = lax.dynamic_index_in_dim(integrals, send_at, 0, keepdims=False)
    perm = [(v, (v + half) % n_virt) for v in range(n_virt)]
    recv_int = lax.ppermute(send_int, "virt", perm)
    recv_amp = lax.ppermute(send_amp, "virt", perm)

    def own_amps(slot):
        return symmetric_amps(amplitudes[slot], tile_flags[slot])

    first_two = lax.all_gather(integrals[0:2], "pair", axis=1, tiled=True)
    running = tile_product(own_amps(0), first_two[0], lax.Precision.HIGHEST)
    second = tile_product(own_amps(1), first_two[1], lax.Precision.HIGHEST)
    running = running + jnp.where(keep > 1, second, jnp.zeros_like(second))

    third_int = jnp.where(take > 0, recv_int, integrals[2])
    third_amp = jnp.where(take > 0, recv_amp, own_amps(2))
    third = tile_product(third_amp, lax.all_gather(third_int, "pair", axis=0, tiled=True))
    third_live = (take > 0) | (keep > 2)
    running = running + jnp.where(third_live, third, jnp.zeros_like(third))

    def fourth(acc):
        gathered = lax.all_gather(integrals[3], "pair", axis=0, tiled=True)
        term = tile_product(own_amps(3), gathered)
        return acc + jnp.where(keep > 3, term, jnp.zeros_like(term))

    all_counts = live_count
    all_partners = jnp.roll(live_count, half)
    all_keep = all_counts - jnp.clip((all_counts - all_partners) // 2, 0, 1)
    any_full = jnp.max(all_keep) > 3
    running = lax.cond(any_full, fourth, lambda acc: acc, running)

    ab = running.shape[1]
    blocks = running.reshape(n_virt, pair_rows // n_virt, ab)
    received = lax.all_to_all(blocks, "virt", 0, 0, tiled=False)
    ladder = jnp.sum(received, axis=0)

    occ_range = jnp.arange(occ_energy.shape[0], dtype=jnp.int32)
    first_energy = jnp.sum(
        jnp.where(pair_occ[:, 0:1] == occ_range[None, :], occ_energy[None, :], 0.0), axis=1
    )
    second_energy = jnp.sum(
        jnp.where(pair_occ[:, 1:2] == occ_range[None, :], occ_energy[None, :], 0.0), axis=1
    )
    denominator = ab_energy[None, :] - first_energy[:, None] - second_energy[:, None]
    return (ladder, ladder / denominator)


def solution(mesh):
    return jax.shard_map(
        on_device,
        mesh=mesh,
        in_specs=(
            P("virt", "pair", None),
            P("virt", "pair", None),
            P("virt"),
            P(),
            P(("pair", "virt"), None),
            P(),
            P(),
        ),
        out_specs=(P(("pair", "virt"), None), P(("pair", "virt"), None)),
        check_vma=False,
    )
```

```python
import jax
import jax.numpy as jnp
from jax import lax
from jax.sharding import PartitionSpec as P

TILE = 64


def swap_in_tile(rows):
    shaped = rows.reshape(rows.shape[0], TILE, TILE)
    return jnp.swapaxes(shaped, 1, 2).reshape(rows.shape)


def symmetric_amps(amp_rows, flag):
    return amp_rows + flag.astype(jnp.float32) * swap_in_tile(amp_rows)


def tile_product(amp_tile, int_rows, precision=lax.Precision.HIGH):
    return lax.dot_general(
        amp_tile,
        int_rows,
        (((1,), (1,)), ((), ())),
        precision=precision,
        preferred_element_type=jnp.float32,
    )


def on_device(amplitudes, integrals, tile_flags, live_count, pair_occ, occ_energy, ab_energy):
    slots, pair_rows, _ = amplitudes.shape
    n_virt = lax.axis_size("virt")
    half = n_virt // 2
    virt_index = lax.axis_index("virt")
    partner = (virt_index + half) % n_virt
    columns = jnp.arange(n_virt, dtype=jnp.int32)
    neighbour = columns ^ 1
    across = jnp.roll(live_count, half)
    give_one = jnp.clip((live_count - across) // 2, 0, 1)
    take_one = jnp.clip((across - live_count) // 2, 0, 1)
    keep_one = live_count - give_one
    give_two = (
        (keep_one == 4) & (take_one[neighbour] == 0) & (keep_one[neighbour] <= 2)
    ).astype(jnp.int32)
    take_two = give_two[neighbour]
    keep_all = keep_one - give_two
    own_count = live_count[virt_index]
    take = take_one[virt_index]
    take_y = take_two[virt_index]
    keep = keep_all[virt_index]

    send_at = own_count - 1
    send_amp = symmetric_amps(
        lax.dynamic_index_in_dim(amplitudes, send_at, 0, keepdims=False),
        lax.dynamic_index_in_dim(tile_flags, send_at, 0, keepdims=False),
    )
    send_int = lax.dynamic_index_in_dim(integrals, send_at, 0, keepdims=False)
    perm = [(v, (v + half) % n_virt) for v in range(n_virt)]
    recv_int = lax.ppermute(send_int, "virt", perm)
    recv_amp = lax.ppermute(send_amp, "virt", perm)
    perm_y = [(v, v ^ 1) for v in range(n_virt)]
    recv_int_y = lax.ppermute(integrals[3], "virt", perm_y)
    recv_amp_y = lax.ppermute(symmetric_amps(amplitudes[3], tile_flags[3]), "virt", perm_y)

    def own_amps(slot):
        return symmetric_amps(amplitudes[slot], tile_flags[slot])

    first_two = lax.all_gather(integrals[0:2], "pair", axis=1, tiled=True)
    running = tile_product(own_amps(0), first_two[0], lax.Precision.HIGHEST)
    second = tile_product(own_amps(1), first_two[1], lax.Precision.HIGHEST)
    running = running + jnp.where(keep > 1, second, jnp.zeros_like(second))

    third_int = jnp.where(take > 0, recv_int, jnp.where(take_y > 0, recv_int_y, integrals[2]))
    third_amp = jnp.where(take > 0, recv_amp, jnp.where(take_y > 0, recv_amp_y, own_amps(2)))
    third = tile_product(third_amp, lax.all_gather(third_int, "pair", axis=0, tiled=True))
    third_live = (take > 0) | (take_y > 0) | (keep > 2)
    running = running + jnp.where(third_live, third, jnp.zeros_like(third))

    def fourth(acc):
        gathered = lax.all_gather(integrals[3], "pair", axis=0, tiled=True)
        term = tile_product(own_amps(3), gathered)
        return acc + jnp.where(keep > 3, term, jnp.zeros_like(term))

    any_full = jnp.max(keep_all) > 3
    running = lax.cond(any_full, fourth, lambda acc: acc, running)

    ab = running.shape[1]
    blocks = running.reshape(n_virt, pair_rows // n_virt, ab)
    received = lax.all_to_all(blocks, "virt", 0, 0, tiled=False)
    ladder = jnp.sum(received, axis=0)

    occ_range = jnp.arange(occ_energy.shape[0], dtype=jnp.int32)
    first_energy = jnp.sum(
        jnp.where(pair_occ[:, 0:1] == occ_range[None, :], occ_energy[None, :], 0.0), axis=1
    )
    second_energy = jnp.sum(
        jnp.where(pair_occ[:, 1:2] == occ_range[None, :], occ_energy[None, :], 0.0), axis=1
    )
    denominator = ab_energy[None, :] - first_energy[:, None] - second_energy[:, None]
    return (ladder, ladder / denominator)


def solution(mesh):
    return jax.shard_map(
        on_device,
        mesh=mesh,
        in_specs=(
            P("virt", "pair", None),
            P("virt", "pair", None),
            P("virt"),
            P(),
            P(("pair", "virt"), None),
            P(),
            P(),
        ),
        out_specs=(P(("pair", "virt"), None), P(("pair", "virt"), None)),
        check_vma=False,
    )
```

```python
import jax
import jax.numpy as jnp
from jax import lax
from jax.sharding import PartitionSpec as P

TILE = 64


def swap_in_tile(rows):
    shaped = rows.reshape(rows.shape[0], TILE, TILE)
    return jnp.swapaxes(shaped, 1, 2).reshape(rows.shape)


def symmetric_amps(amp_rows, flag):
    return amp_rows + flag.astype(jnp.float32) * swap_in_tile(amp_rows)


def tile_product(amp_tile, int_rows, precision=lax.Precision.HIGH):
    return lax.dot_general(
        amp_tile,
        int_rows,
        (((1,), (1,)), ((), ())),
        precision=precision,
        preferred_element_type=jnp.float32,
    )


def on_device(amplitudes, integrals, tile_flags, live_count, pair_occ, occ_energy, ab_energy):
    slots, pair_rows, _ = amplitudes.shape
    n_virt = lax.axis_size("virt")
    half = n_virt // 2
    virt_index = lax.axis_index("virt")
    partner = (virt_index + half) % n_virt
    columns = jnp.arange(n_virt, dtype=jnp.int32)
    neighbour = columns ^ 1
    across = jnp.roll(live_count, half)
    give_one = jnp.clip((live_count - across) // 2, 0, 1)
    take_one = jnp.clip((across - live_count) // 2, 0, 1)
    keep_one = live_count - give_one
    give_two = (
        (keep_one == 4) & (take_one[neighbour] == 0) & (keep_one[neighbour] <= 2)
    ).astype(jnp.int32)
    take_two = give_two[neighbour]
    keep_all = keep_one - give_two
    own_count = live_count[virt_index]
    take = take_one[virt_index]
    take_y = take_two[virt_index]
    keep = keep_all[virt_index]

    send_at = own_count - 1
    send_amp = symmetric_amps(
        lax.dynamic_index_in_dim(amplitudes, send_at, 0, keepdims=False),
        lax.dynamic_index_in_dim(tile_flags, send_at, 0, keepdims=False),
    )
    send_int = lax.dynamic_index_in_dim(integrals, send_at, 0, keepdims=False)
    perm = [(v, (v + half) % n_virt) for v in range(n_virt)]
    recv_int = lax.ppermute(send_int, "virt", perm)
    recv_amp = lax.ppermute(send_amp, "virt", perm)
    perm_y = [(v, v ^ 1) for v in range(n_virt)]
    recv_int_y = lax.ppermute(integrals[3], "virt", perm_y)
    recv_amp_y = lax.ppermute(symmetric_amps(amplitudes[3], tile_flags[3]), "virt", perm_y)

    def own_amps(slot):
        return symmetric_amps(amplitudes[slot], tile_flags[slot])

    first_two = lax.all_gather(integrals[0:2], "pair", axis=1, tiled=True)
    running = tile_product(own_amps(0), first_two[0], lax.Precision.HIGHEST)
    second = tile_product(own_amps(1), first_two[1], lax.Precision.HIGHEST)
    running = running + jnp.where(keep > 1, second, jnp.zeros_like(second))

    third_int = jnp.where(take > 0, recv_int, jnp.where(take_y > 0, recv_int_y, integrals[2]))
    third_amp = jnp.where(take > 0, recv_amp, jnp.where(take_y > 0, recv_amp_y, own_amps(2)))
    third = tile_product(third_amp, lax.all_gather(third_int, "pair", axis=0, tiled=True))
    third_live = (take > 0) | (take_y > 0) | (keep > 2)
    running = running + jnp.where(third_live, third, jnp.zeros_like(third))

    def fourth(acc):
        gathered = lax.all_gather(integrals[3], "pair", axis=0, tiled=True)
        term = tile_product(own_amps(3), gathered)
        return acc + jnp.where(keep > 3, term, jnp.zeros_like(term))

    any_full = jnp.max(keep_all) > 3
    running = lax.cond(any_full, fourth, lambda acc: acc, running)

    ab = running.shape[1]
    side = 4
    along_x = [[y + side * x for x in range(n_virt // side)] for y in range(side)]
    along_y = [[side * x + y for y in range(side)] for x in range(n_virt // side)]
    first = running.reshape(n_virt // side, pair_rows // (n_virt // side), ab)
    first = jnp.sum(lax.all_to_all(first, "virt", 0, 0, axis_index_groups=along_x), axis=0)
    second = first.reshape(side, first.shape[0] // side, ab)
    ladder = jnp.sum(lax.all_to_all(second, "virt", 0, 0, axis_index_groups=along_y), axis=0)

    occ_range = jnp.arange(occ_energy.shape[0], dtype=jnp.int32)
    first_energy = jnp.sum(
        jnp.where(pair_occ[:, 0:1] == occ_range[None, :], occ_energy[None, :], 0.0), axis=1
    )
    second_energy = jnp.sum(
        jnp.where(pair_occ[:, 1:2] == occ_range[None, :], occ_energy[None, :], 0.0), axis=1
    )
    denominator = ab_energy[None, :] - first_energy[:, None] - second_energy[:, None]
    return (ladder, ladder / denominator)


def solution(mesh):
    return jax.shard_map(
        on_device,
        mesh=mesh,
        in_specs=(
            P("virt", "pair", None),
            P("virt", "pair", None),
            P("virt"),
            P(),
            P(("pair", "virt"), None),
            P(),
            P(),
        ),
        out_specs=(P(("pair", "virt"), None), P(("pair", "virt"), None)),
        check_vma=False,
    )
```

```python
import jax
import jax.numpy as jnp
from jax import lax
from jax.experimental import pallas as pl
from jax.experimental.pallas import tpu as pltpu
from jax.sharding import PartitionSpec as P

TILE = 64
CHUNK = 1024


def _split(x):
    hi = x.astype(jnp.bfloat16)
    lo = (x - hi.astype(jnp.float32)).astype(jnp.bfloat16)
    return hi, lo


def _three_pass_kernel(init_ref, a_ref, g_ref, o_ref, acc_ref):
    step = pl.program_id(0)

    @pl.when(step == 0)
    def _():
        acc_ref[...] = init_ref[...]

    a_hi, a_lo = _split(a_ref[...])
    g_hi, g_lo = _split(g_ref[...])
    dims = (((1,), (1,)), ((), ()))

    def dot(x, y):
        return lax.dot_general(x, y, dims, preferred_element_type=jnp.float32)

    acc_ref[...] += dot(a_hi, g_hi) + (dot(a_hi, g_lo) + dot(a_lo, g_hi))

    @pl.when(step == pl.num_programs(0) - 1)
    def _():
        o_ref[...] = acc_ref[...]


def three_pass_product(init, amp_tile, int_rows):
    rows, depth = amp_tile.shape
    cols = int_rows.shape[0]
    steps = depth // CHUNK
    return pl.pallas_call(
        _three_pass_kernel,
        grid=(steps,),
        in_specs=[
            pl.BlockSpec((rows, cols), lambda k: (0, 0)),
            pl.BlockSpec((rows, CHUNK), lambda k: (0, k)),
            pl.BlockSpec((cols, CHUNK), lambda k: (0, k)),
        ],
        out_specs=pl.BlockSpec((rows, cols), lambda k: (0, 0)),
        out_shape=jax.ShapeDtypeStruct((rows, cols), jnp.float32),
        scratch_shapes=[pltpu.VMEM((rows, cols), jnp.float32)],
        compiler_params=pltpu.CompilerParams(dimension_semantics=("arbitrary",)),
        cost_estimate=pl.CostEstimate(
            flops=6 * rows * cols * depth,
            bytes_accessed=4 * (rows * depth + cols * depth + 2 * rows * cols),
            transcendentals=0,
        ),
    )(init, amp_tile, int_rows)


def swap_in_tile(rows):
    shaped = rows.reshape(rows.shape[0], TILE, TILE)
    return jnp.swapaxes(shaped, 1, 2).reshape(rows.shape)


def symmetric_amps(amp_rows, flag):
    return amp_rows + flag.astype(jnp.float32) * swap_in_tile(amp_rows)


def tile_product(amp_tile, int_rows, precision=lax.Precision.HIGH):
    return lax.dot_general(
        amp_tile,
        int_rows,
        (((1,), (1,)), ((), ())),
        precision=precision,
        preferred_element_type=jnp.float32,
    )


def on_device(amplitudes, integrals, tile_flags, live_count, pair_occ, occ_energy, ab_energy):
    slots, pair_rows, _ = amplitudes.shape
    n_virt = lax.axis_size("virt")
    half = n_virt // 2
    virt_index = lax.axis_index("virt")
    partner = (virt_index + half) % n_virt
    columns = jnp.arange(n_virt, dtype=jnp.int32)
    neighbour = columns ^ 1
    across = jnp.roll(live_count, half)
    give_one = jnp.clip((live_count - across) // 2, 0, 1)
    take_one = jnp.clip((across - live_count) // 2, 0, 1)
    keep_one = live_count - give_one
    give_two = (
        (keep_one == 4) & (take_one[neighbour] == 0) & (keep_one[neighbour] <= 2)
    ).astype(jnp.int32)
    take_two = give_two[neighbour]
    keep_all = keep_one - give_two
    own_count = live_count[virt_index]
    take = take_one[virt_index]
    take_y = take_two[virt_index]
    keep = keep_all[virt_index]

    send_at = own_count - 1
    send_amp = symmetric_amps(
        lax.dynamic_index_in_dim(amplitudes, send_at, 0, keepdims=False),
        lax.dynamic_index_in_dim(tile_flags, send_at, 0, keepdims=False),
    )
    send_int = lax.dynamic_index_in_dim(integrals, send_at, 0, keepdims=False)
    perm = [(v, (v + half) % n_virt) for v in range(n_virt)]
    recv_int = lax.ppermute(send_int, "virt", perm)
    recv_amp = lax.ppermute(send_amp, "virt", perm)
    perm_y = [(v, v ^ 1) for v in range(n_virt)]
    recv_int_y = lax.ppermute(integrals[3], "virt", perm_y)
    recv_amp_y = lax.ppermute(symmetric_amps(amplitudes[3], tile_flags[3]), "virt", perm_y)

    def own_amps(slot):
        return symmetric_amps(amplitudes[slot], tile_flags[slot])

    first_two = lax.all_gather(integrals[0:2], "pair", axis=1, tiled=True)
    running = tile_product(own_amps(0), first_two[0], lax.Precision.HIGHEST)
    second = tile_product(own_amps(1), first_two[1], lax.Precision.HIGHEST)
    running = running + jnp.where(keep > 1, second, jnp.zeros_like(second))

    third_int = jnp.where(take > 0, recv_int, jnp.where(take_y > 0, recv_int_y, integrals[2]))
    third_amp = jnp.where(take > 0, recv_amp, jnp.where(take_y > 0, recv_amp_y, own_amps(2)))
    third_live = (take > 0) | (take_y > 0) | (keep > 2)
    third_amp = jnp.where(third_live, third_amp, jnp.zeros_like(third_amp))
    running = three_pass_product(
        running, third_amp, lax.all_gather(third_int, "pair", axis=0, tiled=True)
    )

    def fourth(acc):
        gathered = lax.all_gather(integrals[3], "pair", axis=0, tiled=True)
        term = tile_product(own_amps(3), gathered)
        return acc + jnp.where(keep > 3, term, jnp.zeros_like(term))

    any_full = jnp.max(keep_all) > 3
    running = lax.cond(any_full, fourth, lambda acc: acc, running)

    ab = running.shape[1]
    blocks = running.reshape(n_virt, pair_rows // n_virt, ab)
    received = lax.all_to_all(blocks, "virt", 0, 0, tiled=False)
    ladder = jnp.sum(received, axis=0)

    occ_range = jnp.arange(occ_energy.shape[0], dtype=jnp.int32)
    first_energy = jnp.sum(
        jnp.where(pair_occ[:, 0:1] == occ_range[None, :], occ_energy[None, :], 0.0), axis=1
    )
    second_energy = jnp.sum(
        jnp.where(pair_occ[:, 1:2] == occ_range[None, :], occ_energy[None, :], 0.0), axis=1
    )
    denominator = ab_energy[None, :] - first_energy[:, None] - second_energy[:, None]
    return (ladder, ladder / denominator)


def solution(mesh):
    return jax.shard_map(
        on_device,
        mesh=mesh,
        in_specs=(
            P("virt", "pair", None),
            P("virt", "pair", None),
            P("virt"),
            P(),
            P(("pair", "virt"), None),
            P(),
            P(),
        ),
        out_specs=(P(("pair", "virt"), None), P(("pair", "virt"), None)),
        check_vma=False,
    )
```

```python
import jax
import jax.numpy as jnp
from jax import lax
from jax.experimental import pallas as pl
from jax.experimental.pallas import tpu as pltpu
from jax.sharding import PartitionSpec as P

TILE = 64
CHUNK = 1024


def _split(x):
    hi = x.astype(jnp.bfloat16)
    lo = (x - hi.astype(jnp.float32)).astype(jnp.bfloat16)
    return hi, lo


def _three_pass_kernel(init_ref, a_ref, g_ref, o_ref, acc_ref):
    step = pl.program_id(0)

    @pl.when(step == 0)
    def _():
        acc_ref[...] = init_ref[...]

    a_hi, a_lo = _split(a_ref[...])
    g_hi, g_lo = _split(g_ref[...])
    dims = (((1,), (1,)), ((), ()))

    def dot(x, y):
        return lax.dot_general(x, y, dims, preferred_element_type=jnp.float32)

    acc_ref[...] += dot(a_hi, g_hi) + (dot(a_hi, g_lo) + dot(a_lo, g_hi))

    @pl.when(step == pl.num_programs(0) - 1)
    def _():
        o_ref[...] = acc_ref[...]


def three_pass_product(init, amp_tile, int_rows):
    rows, depth = amp_tile.shape
    cols = int_rows.shape[0]
    steps = depth // CHUNK
    return pl.pallas_call(
        _three_pass_kernel,
        grid=(steps,),
        in_specs=[
            pl.BlockSpec((rows, cols), lambda k: (0, 0)),
            pl.BlockSpec((rows, CHUNK), lambda k: (0, k)),
            pl.BlockSpec((cols, CHUNK), lambda k: (0, k)),
        ],
        out_specs=pl.BlockSpec((rows, cols), lambda k: (0, 0)),
        out_shape=jax.ShapeDtypeStruct((rows, cols), jnp.float32),
        scratch_shapes=[pltpu.VMEM((rows, cols), jnp.float32)],
        compiler_params=pltpu.CompilerParams(dimension_semantics=("arbitrary",)),
        cost_estimate=pl.CostEstimate(
            flops=6 * rows * cols * depth,
            bytes_accessed=4 * (rows * depth + cols * depth + 2 * rows * cols),
            transcendentals=0,
        ),
    )(init, amp_tile, int_rows)


def swap_in_tile(rows):
    shaped = rows.reshape(rows.shape[0], TILE, TILE)
    return jnp.swapaxes(shaped, 1, 2).reshape(rows.shape)


def symmetric_amps(amp_rows, flag):
    return amp_rows + flag.astype(jnp.float32) * swap_in_tile(amp_rows)


def tile_product(amp_tile, int_rows, precision=lax.Precision.HIGH):
    return lax.dot_general(
        amp_tile,
        int_rows,
        (((1,), (1,)), ((), ())),
        precision=precision,
        preferred_element_type=jnp.float32,
    )


def on_device(amplitudes, integrals, tile_flags, live_count, pair_occ, occ_energy, ab_energy):
    slots, pair_rows, _ = amplitudes.shape
    n_virt = lax.axis_size("virt")
    half = n_virt // 2
    virt_index = lax.axis_index("virt")
    partner = (virt_index + half) % n_virt
    columns = jnp.arange(n_virt, dtype=jnp.int32)
    neighbour = columns ^ 1
    across = jnp.roll(live_count, half)
    give_one = jnp.clip((live_count - across) // 2, 0, 1)
    take_one = jnp.clip((across - live_count) // 2, 0, 1)
    keep_one = live_count - give_one
    give_two = (
        (keep_one == 4) & (take_one[neighbour] == 0) & (keep_one[neighbour] <= 2)
    ).astype(jnp.int32)
    take_two = give_two[neighbour]
    keep_all = keep_one - give_two
    own_count = live_count[virt_index]
    take = take_one[virt_index]
    take_y = take_two[virt_index]
    keep = keep_all[virt_index]

    send_at = own_count - 1
    send_amp = symmetric_amps(
        lax.dynamic_index_in_dim(amplitudes, send_at, 0, keepdims=False),
        lax.dynamic_index_in_dim(tile_flags, send_at, 0, keepdims=False),
    )
    send_int = lax.dynamic_index_in_dim(integrals, send_at, 0, keepdims=False)
    perm = [(v, (v + half) % n_virt) for v in range(n_virt)]
    recv_int = lax.ppermute(send_int, "virt", perm)
    recv_amp = lax.ppermute(send_amp, "virt", perm)
    perm_y = [(v, v ^ 1) for v in range(n_virt)]
    recv_int_y = lax.ppermute(integrals[3], "virt", perm_y)
    recv_amp_y = lax.ppermute(symmetric_amps(amplitudes[3], tile_flags[3]), "virt", perm_y)

    def own_amps(slot):
        return symmetric_amps(amplitudes[slot], tile_flags[slot])

    first_two = lax.all_gather(integrals[0:2], "pair", axis=1, tiled=True)
    second_amp = own_amps(1)
    second_amp = jnp.where(keep > 1, second_amp, jnp.zeros_like(second_amp))
    running = three_pass_product(
        jnp.zeros((pair_rows, first_two.shape[1]), jnp.float32), own_amps(0), first_two[0]
    )
    running = three_pass_product(running, second_amp, first_two[1])

    third_int = jnp.where(take > 0, recv_int, jnp.where(take_y > 0, recv_int_y, integrals[2]))
    third_amp = jnp.where(take > 0, recv_amp, jnp.where(take_y > 0, recv_amp_y, own_amps(2)))
    third_live = (take > 0) | (take_y > 0) | (keep > 2)
    third_amp = jnp.where(third_live, third_amp, jnp.zeros_like(third_amp))
    running = three_pass_product(
        running, third_amp, lax.all_gather(third_int, "pair", axis=0, tiled=True)
    )

    def fourth(acc):
        gathered = lax.all_gather(integrals[3], "pair", axis=0, tiled=True)
        term = tile_product(own_amps(3), gathered)
        return acc + jnp.where(keep > 3, term, jnp.zeros_like(term))

    any_full = jnp.max(keep_all) > 3
    running = lax.cond(any_full, fourth, lambda acc: acc, running)

    ab = running.shape[1]
    blocks = running.reshape(n_virt, pair_rows // n_virt, ab)
    received = lax.all_to_all(blocks, "virt", 0, 0, tiled=False)
    ladder = jnp.sum(received, axis=0)

    occ_range = jnp.arange(occ_energy.shape[0], dtype=jnp.int32)
    first_energy = jnp.sum(
        jnp.where(pair_occ[:, 0:1] == occ_range[None, :], occ_energy[None, :], 0.0), axis=1
    )
    second_energy = jnp.sum(
        jnp.where(pair_occ[:, 1:2] == occ_range[None, :], occ_energy[None, :], 0.0), axis=1
    )
    denominator = ab_energy[None, :] - first_energy[:, None] - second_energy[:, None]
    return (ladder, ladder / denominator)


def solution(mesh):
    return jax.shard_map(
        on_device,
        mesh=mesh,
        in_specs=(
            P("virt", "pair", None),
            P("virt", "pair", None),
            P("virt"),
            P(),
            P(("pair", "virt"), None),
            P(),
            P(),
        ),
        out_specs=(P(("pair", "virt"), None), P(("pair", "virt"), None)),
        check_vma=False,
    )
```

```python
import jax
import jax.numpy as jnp
from jax import lax
from jax.experimental import pallas as pl
from jax.experimental.pallas import tpu as pltpu
from jax.sharding import PartitionSpec as P

TILE = 64
CHUNK = 1024


def _split(x):
    hi = x.astype(jnp.bfloat16)
    lo = (x - hi.astype(jnp.float32)).astype(jnp.bfloat16)
    return hi, lo


def _split_kernel(a_ref, hi_ref, lo_ref):
    hi, lo = _split(a_ref[...])
    hi_ref[...] = hi
    lo_ref[...] = lo


def split_amps(amp_tile):
    rows, depth = amp_tile.shape
    block = pl.BlockSpec((rows, CHUNK), lambda k: (0, k))
    half_type = jax.ShapeDtypeStruct((rows, depth), jnp.bfloat16)
    return pl.pallas_call(
        _split_kernel,
        grid=(depth // CHUNK,),
        in_specs=[block],
        out_specs=[block, block],
        out_shape=[half_type, half_type],
        compiler_params=pltpu.CompilerParams(dimension_semantics=("arbitrary",)),
        cost_estimate=pl.CostEstimate(
            flops=3 * rows * depth, bytes_accessed=8 * rows * depth, transcendentals=0
        ),
    )(amp_tile)


def _three_pass_kernel(init_ref, a_hi_ref, a_lo_ref, g_ref, o_ref, acc_ref):
    step = pl.program_id(0)

    @pl.when(step == 0)
    def _():
        acc_ref[...] = init_ref[...]

    a_hi = a_hi_ref[...]
    g_hi, g_lo = _split(g_ref[...])
    dims = (((1,), (1,)), ((), ()))

    def dot(x, y):
        return lax.dot_general(x, y, dims, preferred_element_type=jnp.float32)

    acc_ref[...] += dot(a_hi, g_hi) + (dot(a_hi, g_lo) + dot(a_lo_ref[...], g_hi))

    @pl.when(step == pl.num_programs(0) - 1)
    def _():
        o_ref[...] = acc_ref[...]


def three_pass_product(init, amp_tile, int_rows):
    rows, depth = amp_tile.shape
    cols = int_rows.shape[0]
    a_hi, a_lo = split_amps(amp_tile)
    amp_block = pl.BlockSpec((rows, CHUNK), lambda k: (0, k))
    return pl.pallas_call(
        _three_pass_kernel,
        grid=(depth // CHUNK,),
        in_specs=[
            pl.BlockSpec((rows, cols), lambda k: (0, 0)),
            amp_block,
            amp_block,
            pl.BlockSpec((cols, CHUNK), lambda k: (0, k)),
        ],
        out_specs=pl.BlockSpec((rows, cols), lambda k: (0, 0)),
        out_shape=jax.ShapeDtypeStruct((rows, cols), jnp.float32),
        scratch_shapes=[pltpu.VMEM((rows, cols), jnp.float32)],
        compiler_params=pltpu.CompilerParams(dimension_semantics=("arbitrary",)),
        cost_estimate=pl.CostEstimate(
            flops=6 * rows * cols * depth,
            bytes_accessed=4 * (rows * depth + cols * depth + 2 * rows * cols),
            transcendentals=0,
        ),
    )(init, a_hi, a_lo, int_rows)


def swap_in_tile(rows):
    shaped = rows.reshape(rows.shape[0], TILE, TILE)
    return jnp.swapaxes(shaped, 1, 2).reshape(rows.shape)


def symmetric_amps(amp_rows, flag):
    return amp_rows + flag.astype(jnp.float32) * swap_in_tile(amp_rows)


def tile_product(amp_tile, int_rows, precision=lax.Precision.HIGH):
    return lax.dot_general(
        amp_tile,
        int_rows,
        (((1,), (1,)), ((), ())),
        precision=precision,
        preferred_element_type=jnp.float32,
    )


def on_device(amplitudes, integrals, tile_flags, live_count, pair_occ, occ_energy, ab_energy):
    slots, pair_rows, _ = amplitudes.shape
    n_virt = lax.axis_size("virt")
    half = n_virt // 2
    virt_index = lax.axis_index("virt")
    partner = (virt_index + half) % n_virt
    columns = jnp.arange(n_virt, dtype=jnp.int32)
    neighbour = columns ^ 1
    across = jnp.roll(live_count, half)
    give_one = jnp.clip((live_count - across) // 2, 0, 1)
    take_one = jnp.clip((across - live_count) // 2, 0, 1)
    keep_one = live_count - give_one
    give_two = (
        (keep_one == 4) & (take_one[neighbour] == 0) & (keep_one[neighbour] <= 2)
    ).astype(jnp.int32)
    take_two = give_two[neighbour]
    keep_all = keep_one - give_two
    own_count = live_count[virt_index]
    take = take_one[virt_index]
    take_y = take_two[virt_index]
    keep = keep_all[virt_index]

    send_at = own_count - 1
    send_amp = symmetric_amps(
        lax.dynamic_index_in_dim(amplitudes, send_at, 0, keepdims=False),
        lax.dynamic_index_in_dim(tile_flags, send_at, 0, keepdims=False),
    )
    send_int = lax.dynamic_index_in_dim(integrals, send_at, 0, keepdims=False)
    perm = [(v, (v + half) % n_virt) for v in range(n_virt)]
    recv_int = lax.ppermute(send_int, "virt", perm)
    recv_amp = lax.ppermute(send_amp, "virt", perm)
    perm_y = [(v, v ^ 1) for v in range(n_virt)]
    recv_int_y = lax.ppermute(integrals[3], "virt", perm_y)
    recv_amp_y = lax.ppermute(symmetric_amps(amplitudes[3], tile_flags[3]), "virt", perm_y)

    def own_amps(slot):
        return symmetric_amps(amplitudes[slot], tile_flags[slot])

    first_two = lax.all_gather(integrals[0:2], "pair", axis=1, tiled=True)
    running = tile_product(own_amps(0), first_two[0], lax.Precision.HIGHEST)
    second = tile_product(own_amps(1), first_two[1], lax.Precision.HIGHEST)
    running = running + jnp.where(keep > 1, second, jnp.zeros_like(second))

    third_int = jnp.where(take > 0, recv_int, jnp.where(take_y > 0, recv_int_y, integrals[2]))
    third_amp = jnp.where(take > 0, recv_amp, jnp.where(take_y > 0, recv_amp_y, own_amps(2)))
    third_live = (take > 0) | (take_y > 0) | (keep > 2)
    third_amp = jnp.where(third_live, third_amp, jnp.zeros_like(third_amp))
    running = three_pass_product(
        running, third_amp, lax.all_gather(third_int, "pair", axis=0, tiled=True)
    )

    def fourth(acc):
        gathered = lax.all_gather(integrals[3], "pair", axis=0, tiled=True)
        term = tile_product(own_amps(3), gathered)
        return acc + jnp.where(keep > 3, term, jnp.zeros_like(term))

    any_full = jnp.max(keep_all) > 3
    running = lax.cond(any_full, fourth, lambda acc: acc, running)

    ab = running.shape[1]
    blocks = running.reshape(n_virt, pair_rows // n_virt, ab)
    received = lax.all_to_all(blocks, "virt", 0, 0, tiled=False)
    ladder = jnp.sum(received, axis=0)

    occ_range = jnp.arange(occ_energy.shape[0], dtype=jnp.int32)
    first_energy = jnp.sum(
        jnp.where(pair_occ[:, 0:1] == occ_range[None, :], occ_energy[None, :], 0.0), axis=1
    )
    second_energy = jnp.sum(
        jnp.where(pair_occ[:, 1:2] == occ_range[None, :], occ_energy[None, :], 0.0), axis=1
    )
    denominator = ab_energy[None, :] - first_energy[:, None] - second_energy[:, None]
    return (ladder, ladder / denominator)


def solution(mesh):
    return jax.shard_map(
        on_device,
        mesh=mesh,
        in_specs=(
            P("virt", "pair", None),
            P("virt", "pair", None),
            P("virt"),
            P(),
            P(("pair", "virt"), None),
            P(),
            P(),
        ),
        out_specs=(P(("pair", "virt"), None), P(("pair", "virt"), None)),
        check_vma=False,
    )
```

```python
import jax
import jax.numpy as jnp
from jax import lax
from jax.experimental import pallas as pl
from jax.experimental.pallas import tpu as pltpu
from jax.sharding import PartitionSpec as P

TILE = 64
CHUNK = 512


def _split(x):
    hi = x.astype(jnp.bfloat16)
    lo = (x - hi.astype(jnp.float32)).astype(jnp.bfloat16)
    return hi, lo


def _three_pass_kernel(init_ref, a_ref, g_ref, o_ref, acc_ref):
    step = pl.program_id(0)

    @pl.when(step == 0)
    def _():
        acc_ref[...] = init_ref[...]

    a_hi, a_lo = _split(a_ref[...])
    g_hi, g_lo = _split(g_ref[...])
    dims = (((1,), (1,)), ((), ()))

    def dot(x, y):
        return lax.dot_general(x, y, dims, preferred_element_type=jnp.float32)

    acc_ref[...] += dot(a_hi, g_hi) + (dot(a_hi, g_lo) + dot(a_lo, g_hi))

    @pl.when(step == pl.num_programs(0) - 1)
    def _():
        o_ref[...] = acc_ref[...]


def three_pass_product(init, amp_tile, int_rows):
    rows, depth = amp_tile.shape
    cols = int_rows.shape[0]
    steps = depth // CHUNK
    return pl.pallas_call(
        _three_pass_kernel,
        grid=(steps,),
        in_specs=[
            pl.BlockSpec((rows, cols), lambda k: (0, 0)),
            pl.BlockSpec((rows, CHUNK), lambda k: (0, k)),
            pl.BlockSpec((cols, CHUNK), lambda k: (0, k)),
        ],
        out_specs=pl.BlockSpec((rows, cols), lambda k: (0, 0)),
        out_shape=jax.ShapeDtypeStruct((rows, cols), jnp.float32),
        scratch_shapes=[pltpu.VMEM((rows, cols), jnp.float32)],
        compiler_params=pltpu.CompilerParams(dimension_semantics=("arbitrary",)),
        cost_estimate=pl.CostEstimate(
            flops=6 * rows * cols * depth,
            bytes_accessed=4 * (rows * depth + cols * depth + 2 * rows * cols),
            transcendentals=0,
        ),
    )(init, amp_tile, int_rows)


def swap_in_tile(rows):
    shaped = rows.reshape(rows.shape[0], TILE, TILE)
    return jnp.swapaxes(shaped, 1, 2).reshape(rows.shape)


def symmetric_amps(amp_rows, flag):
    return amp_rows + flag.astype(jnp.float32) * swap_in_tile(amp_rows)


def tile_product(amp_tile, int_rows, precision=lax.Precision.HIGH):
    return lax.dot_general(
        amp_tile,
        int_rows,
        (((1,), (1,)), ((), ())),
        precision=precision,
        preferred_element_type=jnp.float32,
    )


def on_device(amplitudes, integrals, tile_flags, live_count, pair_occ, occ_energy, ab_energy):
    slots, pair_rows, _ = amplitudes.shape
    n_virt = lax.axis_size("virt")
    half = n_virt // 2
    virt_index = lax.axis_index("virt")
    partner = (virt_index + half) % n_virt
    columns = jnp.arange(n_virt, dtype=jnp.int32)
    neighbour = columns ^ 1
    across = jnp.roll(live_count, half)
    give_one = jnp.clip((live_count - across) // 2, 0, 1)
    take_one = jnp.clip((across - live_count) // 2, 0, 1)
    keep_one = live_count - give_one
    give_two = (
        (keep_one == 4) & (take_one[neighbour] == 0) & (keep_one[neighbour] <= 2)
    ).astype(jnp.int32)
    take_two = give_two[neighbour]
    keep_all = keep_one - give_two
    own_count = live_count[virt_index]
    take = take_one[virt_index]
    take_y = take_two[virt_index]
    keep = keep_all[virt_index]

    send_at = own_count - 1
    send_amp = symmetric_amps(
        lax.dynamic_index_in_dim(amplitudes, send_at, 0, keepdims=False),
        lax.dynamic_index_in_dim(tile_flags, send_at, 0, keepdims=False),
    )
    send_int = lax.dynamic_index_in_dim(integrals, send_at, 0, keepdims=False)
    perm = [(v, (v + half) % n_virt) for v in range(n_virt)]
    recv_int = lax.ppermute(send_int, "virt", perm)
    recv_amp = lax.ppermute(send_amp, "virt", perm)
    perm_y = [(v, v ^ 1) for v in range(n_virt)]
    recv_int_y = lax.ppermute(integrals[3], "virt", perm_y)
    recv_amp_y = lax.ppermute(symmetric_amps(amplitudes[3], tile_flags[3]), "virt", perm_y)

    def own_amps(slot):
        return symmetric_amps(amplitudes[slot], tile_flags[slot])

    first_two = lax.all_gather(integrals[0:2], "pair", axis=1, tiled=True)
    running = tile_product(own_amps(0), first_two[0], lax.Precision.HIGHEST)
    second = tile_product(own_amps(1), first_two[1], lax.Precision.HIGHEST)
    running = running + jnp.where(keep > 1, second, jnp.zeros_like(second))

    third_int = jnp.where(take > 0, recv_int, jnp.where(take_y > 0, recv_int_y, integrals[2]))
    third_amp = jnp.where(take > 0, recv_amp, jnp.where(take_y > 0, recv_amp_y, own_amps(2)))
    third_live = (take > 0) | (take_y > 0) | (keep > 2)
    third_amp = jnp.where(third_live, third_amp, jnp.zeros_like(third_amp))
    running = three_pass_product(
        running, third_amp, lax.all_gather(third_int, "pair", axis=0, tiled=True)
    )

    def fourth(acc):
        gathered = lax.all_gather(integrals[3], "pair", axis=0, tiled=True)
        term = tile_product(own_amps(3), gathered)
        return acc + jnp.where(keep > 3, term, jnp.zeros_like(term))

    any_full = jnp.max(keep_all) > 3
    running = lax.cond(any_full, fourth, lambda acc: acc, running)

    ab = running.shape[1]
    blocks = running.reshape(n_virt, pair_rows // n_virt, ab)
    received = lax.all_to_all(blocks, "virt", 0, 0, tiled=False)
    ladder = jnp.sum(received, axis=0)

    occ_range = jnp.arange(occ_energy.shape[0], dtype=jnp.int32)
    first_energy = jnp.sum(
        jnp.where(pair_occ[:, 0:1] == occ_range[None, :], occ_energy[None, :], 0.0), axis=1
    )
    second_energy = jnp.sum(
        jnp.where(pair_occ[:, 1:2] == occ_range[None, :], occ_energy[None, :], 0.0), axis=1
    )
    denominator = ab_energy[None, :] - first_energy[:, None] - second_energy[:, None]
    return (ladder, ladder / denominator)


def solution(mesh):
    return jax.shard_map(
        on_device,
        mesh=mesh,
        in_specs=(
            P("virt", "pair", None),
            P("virt", "pair", None),
            P("virt"),
            P(),
            P(("pair", "virt"), None),
            P(),
            P(),
        ),
        out_specs=(P(("pair", "virt"), None), P(("pair", "virt"), None)),
        check_vma=False,
    )
```

```python
import jax
import jax.numpy as jnp
from jax import lax
from jax.experimental import pallas as pl
from jax.experimental.pallas import tpu as pltpu
from jax.sharding import PartitionSpec as P

TILE = 64
CHUNK = 1024


def _split(x):
    hi = x.astype(jnp.bfloat16)
    lo = (x - hi.astype(jnp.float32)).astype(jnp.bfloat16)
    return hi, lo


def _three_pass_kernel(init_ref, a_ref, g_ref, o_ref, acc_ref):
    step = pl.program_id(0)

    @pl.when(step == 0)
    def _():
        acc_ref[...] = init_ref[...]

    a_hi, a_lo = _split(a_ref[...])
    g_hi, g_lo = _split(g_ref[...])
    dims = (((1,), (1,)), ((), ()))

    def dot(x, y):
        return lax.dot_general(x, y, dims, preferred_element_type=jnp.float32)

    acc_ref[...] += dot(a_hi, g_hi) + (dot(a_hi, g_lo) + dot(a_lo, g_hi))

    @pl.when(step == pl.num_programs(0) - 1)
    def _():
        o_ref[...] = acc_ref[...]


def three_pass_product(init, amp_tile, int_rows):
    rows, depth = amp_tile.shape
    cols = int_rows.shape[0]
    steps = depth // CHUNK
    return pl.pallas_call(
        _three_pass_kernel,
        grid=(steps,),
        in_specs=[
            pl.BlockSpec((rows, cols), lambda k: (0, 0)),
            pl.BlockSpec((rows, CHUNK), lambda k: (0, k)),
            pl.BlockSpec((cols, CHUNK), lambda k: (0, k)),
        ],
        out_specs=pl.BlockSpec((rows, cols), lambda k: (0, 0)),
        out_shape=jax.ShapeDtypeStruct((rows, cols), jnp.float32),
        scratch_shapes=[pltpu.VMEM((rows, cols), jnp.float32)],
        compiler_params=pltpu.CompilerParams(dimension_semantics=("arbitrary",)),
        cost_estimate=pl.CostEstimate(
            flops=6 * rows * cols * depth,
            bytes_accessed=4 * (rows * depth + cols * depth + 2 * rows * cols),
            transcendentals=0,
        ),
    )(init, amp_tile, int_rows)


def swap_in_tile(rows):
    shaped = rows.reshape(rows.shape[0], TILE, TILE)
    return jnp.swapaxes(shaped, 1, 2).reshape(rows.shape)


def symmetric_amps(amp_rows, flag):
    return amp_rows + flag.astype(jnp.float32) * swap_in_tile(amp_rows)


def tile_product(amp_tile, int_rows, precision=lax.Precision.HIGH):
    return lax.dot_general(
        amp_tile,
        int_rows,
        (((1,), (1,)), ((), ())),
        precision=precision,
        preferred_element_type=jnp.float32,
    )


def on_device(amplitudes, integrals, tile_flags, live_count, pair_occ, occ_energy, ab_energy):
    slots, pair_rows, _ = amplitudes.shape
    n_virt = lax.axis_size("virt")
    half = n_virt // 2
    virt_index = lax.axis_index("virt")
    partner = (virt_index + half) % n_virt
    columns = jnp.arange(n_virt, dtype=jnp.int32)
    neighbour = columns ^ 1
    across = jnp.roll(live_count, half)
    give_one = jnp.clip((live_count - across) // 2, 0, 1)
    take_one = jnp.clip((across - live_count) // 2, 0, 1)
    keep_one = live_count - give_one
    give_two = (
        (keep_one == 4) & (take_one[neighbour] == 0) & (keep_one[neighbour] <= 2)
    ).astype(jnp.int32)
    take_two = give_two[neighbour]
    keep_all = keep_one - give_two
    own_count = live_count[virt_index]
    take = take_one[virt_index]
    take_y = take_two[virt_index]
    keep = keep_all[virt_index]

    send_at = own_count - 1
    send_amp = symmetric_amps(
        lax.dynamic_index_in_dim(amplitudes, send_at, 0, keepdims=False),
        lax.dynamic_index_in_dim(tile_flags, send_at, 0, keepdims=False),
    )
    send_int = lax.dynamic_index_in_dim(integrals, send_at, 0, keepdims=False)
    perm = [(v, (v + half) % n_virt) for v in range(n_virt)]
    recv_int = lax.ppermute(send_int, "virt", perm)
    recv_amp = lax.ppermute(send_amp, "virt", perm)
    perm_y = [(v, v ^ 1) for v in range(n_virt)]
    recv_int_y = lax.ppermute(integrals[3], "virt", perm_y)
    recv_amp_y = lax.ppermute(symmetric_amps(amplitudes[3], tile_flags[3]), "virt", perm_y)

    def own_amps(slot):
        return symmetric_amps(amplitudes[slot], tile_flags[slot])

    first_two = lax.all_gather(integrals[0:2], "pair", axis=1, tiled=True)
    running = tile_product(own_amps(0), first_two[0])
    second = tile_product(own_amps(1), first_two[1])
    running = running + jnp.where(keep > 1, second, jnp.zeros_like(second))

    third_int = jnp.where(take > 0, recv_int, jnp.where(take_y > 0, recv_int_y, integrals[2]))
    third_amp = jnp.where(take > 0, recv_amp, jnp.where(take_y > 0, recv_amp_y, own_amps(2)))
    third_live = (take > 0) | (take_y > 0) | (keep > 2)
    third_amp = jnp.where(third_live, third_amp, jnp.zeros_like(third_amp))
    running = three_pass_product(
        running, third_amp, lax.all_gather(third_int, "pair", axis=0, tiled=True)
    )

    def fourth(acc):
        gathered = lax.all_gather(integrals[3], "pair", axis=0, tiled=True)
        term = tile_product(own_amps(3), gathered)
        return acc + jnp.where(keep > 3, term, jnp.zeros_like(term))

    any_full = jnp.max(keep_all) > 3
    running = lax.cond(any_full, fourth, lambda acc: acc, running)

    ab = running.shape[1]
    blocks = running.reshape(n_virt, pair_rows // n_virt, ab)
    received = lax.all_to_all(blocks, "virt", 0, 0, tiled=False)
    ladder = jnp.sum(received, axis=0)

    occ_range = jnp.arange(occ_energy.shape[0], dtype=jnp.int32)
    first_energy = jnp.sum(
        jnp.where(pair_occ[:, 0:1] == occ_range[None, :], occ_energy[None, :], 0.0), axis=1
    )
    second_energy = jnp.sum(
        jnp.where(pair_occ[:, 1:2] == occ_range[None, :], occ_energy[None, :], 0.0), axis=1
    )
    denominator = ab_energy[None, :] - first_energy[:, None] - second_energy[:, None]
    return (ladder, ladder / denominator)


def solution(mesh):
    return jax.shard_map(
        on_device,
        mesh=mesh,
        in_specs=(
            P("virt", "pair", None),
            P("virt", "pair", None),
            P("virt"),
            P(),
            P(("pair", "virt"), None),
            P(),
            P(),
        ),
        out_specs=(P(("pair", "virt"), None), P(("pair", "virt"), None)),
        check_vma=False,
    )
```
